256 devices in a mesh: grp: 4 (over x), blk: 64 (over z, y, core).
Axes of the slice: x: 4, y: 4, z: 8, core: 2. Of those that a mesh axis runs over, the one named last changes fastest.
Arguments:
- integrals: bfloat16 [4, 64, 10, 24, 128, 128], P('grp', 'blk'), may hold values from -6 to 6
- coefficients: bfloat16 [3072, 192], P('blk'), may hold values from -0.25 to 0.25
- tile_blocks: int32 [4, 64, 10, 2], P('grp', 'blk'), may hold values from 0 to 23
- block_owner: int32 [48], replicated, may hold values from 0 to 3, as said below
Outputs:
- owned: bfloat16 [96, 4, 4, 1536, 192], P('grp', None, None, 'blk')
The draws below stay inside these ranges and needn't reach their ends.
Inputs may be any that keep to these rules, and one draw needn't show every extreme that they name: `block_owner`: each owner holds at most 24 ij blocks, and some owner holds exactly 24.
All inputs are finite; a program needn't handle non-finite values.
Results may differ from the reference program's by a relative error of at most 0.0049.
Values may be sent and summed in bfloat16 or wider, within the bound.
No kernel may reach another device: no remote copies, remote signals or barrier semaphores. Data moves between devices by JAX's collectives and lax.ppermute only.
A program may use at most 64 MiB of HBM per device.

```python
import jax
import jax.numpy as jnp
from jax import lax

NMO = 192
SB = 128
NSH = 24
NBF = 3072
KT = 10
R = 24
IJB = 48
CAP = 24
IPB = 4
N_GRP = 4
N_BLK = 64


def draw_block_owner(key, part):
    key_busy = jax.random.fold_in(key, 11)
    key_perm = jax.random.fold_in(key, 12)
    key_rest = jax.random.fold_in(key, 13)
    busiest = jax.random.randint(key_busy, (), 0, N_GRP).astype(jnp.int32)
    shuffled = jax.random.permutation(key_perm, IJB).astype(jnp.int32)
    position = jnp.argsort(shuffled).astype(jnp.int32)
    others = jax.random.randint(key_rest, (IJB,), 0, N_GRP - 1).astype(jnp.int32)
    others = others + (others >= busiest).astype(jnp.int32)
    return jnp.where(position < CAP, busiest, others).astype(jnp.int32)


def place_ends(drawn, rng, smallest, largest):
    longest = drawn.shape.index(max(drawn.shape))
    spots = []
    for shift in (0, 1):
        where = [jax.random.randint(jax.random.fold_in(rng, axis), (), 0, length) for axis, length in enumerate(drawn.shape)]
        where[longest] = (where[longest] + shift) % drawn.shape[longest]
        spots.append(tuple(where))
    return drawn.at[spots[0]].set(smallest).at[spots[1]].set(largest)


def steps_of(rng, dims, shards, least, high):
    gain = 1.0
    for axis_at, blocks in shards:
        draws = jax.random.uniform(jax.random.fold_in(jax.random.fold_in(rng, 6), axis_at), (blocks,), jnp.float32, least / len(shards), high / len(shards))
        gain = gain * jnp.repeat(jnp.exp(draws), dims[axis_at] // blocks).reshape((-1,) + (1,) * (len(dims) - 1 - axis_at))
    return gain


def normal_values(own_key, dims, deviation, most, pieces=(), kind=jnp.bfloat16):
    result = jax.random.normal(own_key, dims, jnp.float32) * deviation
    if len(pieces) > 0:
        result = steps_of(own_key, dims, pieces, -0.22, 0.18) * result
    return jnp.clip(result, min=-most, max=most).astype(kind)


def setup_inputs(seed: int = 0) -> dict:
    arg_keys = jax.random.split(jax.random.key(seed), 5)
    return {
        "integrals": normal_values(arg_keys[0], (N_GRP, N_BLK, KT, R, SB, SB), 1.0, 6.0, ((0, 4), (1, 64))),
        "coefficients": normal_values(arg_keys[1], (NBF, NMO), (4 * SB) ** -0.5, 0.25, ((0, 64),)),
        "tile_blocks": place_ends(jax.random.randint(arg_keys[2], (N_GRP, N_BLK, KT, 2), 0, NSH), jax.random.fold_in(arg_keys[2], 1), 0, NSH - 1).astype(jnp.int32),
        "block_owner": draw_block_owner(jax.random.fold_in(arg_keys[4], 71), 0),
    }


def slot_table(block_owner, groups, capacity):
    count = block_owner.shape[0]
    order = jnp.arange(count, dtype=jnp.int32)
    same = block_owner[:, None] == block_owner[None, :]
    earlier = order[None, :] < order[:, None]
    rank = jnp.sum((same & earlier).astype(jnp.int32), axis=1).astype(jnp.int32)
    slot = (block_owner * capacity + rank).astype(jnp.int32)
    slots = jnp.arange(groups * capacity, dtype=jnp.int32)
    match = slot[None, :] == slots[:, None]
    source = jnp.sum(jnp.where(match, order[None, :], 0), axis=1).astype(jnp.int32)
    filled = jnp.any(match, axis=1)
    return source, filled


def one_device(args):
    tiles, blocks, panels = args
    la_coef = jnp.take(panels, blocks[:, 0], axis=0).astype(jnp.float32)
    si_coef = jnp.take(panels, blocks[:, 1], axis=0).astype(jnp.float32)
    quarter = jnp.einsum("trab,tbj->tarj", tiles.astype(jnp.float32), si_coef,
                         precision=lax.Precision.HIGHEST).astype(jnp.bfloat16)
    half = jnp.einsum("tai,tarj->irj", la_coef, quarter.astype(jnp.float32),
                      precision=lax.Precision.HIGHEST)
    return half.astype(jnp.bfloat16)


def reference(integrals, coefficients, tile_blocks, block_owner):
    panels = coefficients.reshape(NSH, SB, NMO)
    flat_tiles = integrals.reshape(N_GRP * N_BLK, KT, R, SB, SB)
    flat_blocks = tile_blocks.reshape(N_GRP * N_BLK, KT, 2)
    half_all = lax.map(lambda pair: one_device((pair[0], pair[1], panels)), (flat_tiles, flat_blocks))
    half_all = half_all.reshape(N_GRP, N_BLK, IJB, IPB, R, NMO)
    source, filled = slot_table(block_owner, N_GRP, CAP)
    picked = jnp.take(half_all, source, axis=2)
    picked = jnp.where(filled[None, None, :, None, None, None], picked, jnp.zeros_like(picked))
    picked = jnp.transpose(picked, (2, 0, 3, 1, 4, 5))
    return picked.reshape(N_GRP * CAP, N_GRP, IPB, N_BLK * R, NMO)
```

```python
import numpy as np
import jax
import jax.numpy as jnp
from jax import lax
from jax.sharding import Mesh, PartitionSpec as P

NMO = 192
SB = 128
NSH = 24
R = 24
IJB = 48
CAP = 24
IPB = 4

BLK = ("z", "y", "c")


def slot_table(block_owner, groups, capacity):
    count = block_owner.shape[0]
    order = jnp.arange(count, dtype=jnp.int32)
    same = block_owner[:, None] == block_owner[None, :]
    earlier = order[None, :] < order[:, None]
    rank = jnp.sum((same & earlier).astype(jnp.int32), axis=1)
    slot = block_owner * capacity + rank
    slots = jnp.arange(groups * capacity, dtype=jnp.int32)
    match = slot[None, :] == slots[:, None]
    source = jnp.sum(jnp.where(match, order[None, :], 0), axis=1)
    filled = jnp.any(match, axis=1)
    return (source, filled)


def gather_coef(coefficients):
    x = lax.all_gather(coefficients, "c", axis=0, tiled=True)
    x = lax.all_gather(x, "y", axis=0, tiled=True)
    nz = lax.axis_size("z")
    rep = jnp.broadcast_to(x[None], (nz,) + x.shape)
    return lax.all_to_all(rep, "z", 0, 0, tiled=True).reshape(-1, NMO)


def body(integrals, coefficients, tile_blocks, block_owner):
    groups = lax.axis_size("grp")
    whole_coef = gather_coef(coefficients)
    panels = whole_coef.reshape(NSH, SB, NMO)
    tiles = integrals[0, 0]
    blocks = tile_blocks[0, 0]
    la_coef = jnp.take(panels, blocks[:, 0], axis=0)
    si_coef = jnp.take(panels, blocks[:, 1], axis=0)
    quarter = jnp.einsum(
        "trab,tbj->tarj", tiles, si_coef, preferred_element_type=jnp.float32
    ).astype(jnp.bfloat16)
    half = jnp.einsum("tai,tarj->irj", la_coef, quarter, preferred_element_type=jnp.float32).astype(
        jnp.bfloat16
    )
    pair_blocks = half.reshape(IJB, IPB, R, NMO)
    source, filled = slot_table(block_owner, groups, CAP)
    picked = jnp.take(pair_blocks, source, axis=0)
    picked = jnp.where(filled[:, None, None, None], picked, jnp.zeros_like(picked))
    return lax.all_to_all(picked[:, None], "grp", 0, 1, tiled=True)


def solution(mesh):
    nblk = mesh.shape["blk"]
    devs = np.asarray(mesh.devices).reshape(mesh.shape["grp"], nblk // 8, 4, 2)
    parts = Mesh(devs, ("grp",) + BLK)
    in_specs = (
        P("grp", BLK, None, None, None, None),
        P(BLK, None),
        P("grp", BLK, None, None),
        P(),
    )
    out_specs = P("grp", None, None, BLK, None)
    return jax.shard_map(body, mesh=parts, in_specs=in_specs, out_specs=out_specs, check_vma=False)
```

```python
import numpy as np
import jax
import jax.numpy as jnp
from jax import lax
from jax.sharding import Mesh, PartitionSpec as P

NMO = 192
SB = 128
NSH = 24
R = 24
IJB = 48
CAP = 24
IPB = 4

BLK = ("z", "y", "c")


def slot_table(block_owner, groups, capacity):
    count = block_owner.shape[0]
    order = jnp.arange(count, dtype=jnp.int32)
    same = block_owner[:, None] == block_owner[None, :]
    earlier = order[None, :] < order[:, None]
    rank = jnp.sum((same & earlier).astype(jnp.int32), axis=1)
    slot = block_owner * capacity + rank
    slots = jnp.arange(groups * capacity, dtype=jnp.int32)
    match = slot[None, :] == slots[:, None]
    source = jnp.sum(jnp.where(match, order[None, :], 0), axis=1)
    filled = jnp.any(match, axis=1)
    return (source, filled)


def ring(x, axis):
    n = lax.axis_size(axis)
    got = {0: x}
    f = x
    for k in range(1, n // 2 + 1):
        f = lax.ppermute(f, axis, [(s, (s + 1) % n) for s in range(n)])
        got[-k] = f
    b = x
    for k in range(1, n - n // 2):
        b = lax.ppermute(b, axis, [(s, (s - 1) % n) for s in range(n)])
        got[k] = b
    lo = -(n // 2)
    return jnp.stack([got[o] for o in range(lo, lo + n)]), lo


def gather_coef(coefficients):
    x = lax.all_gather(coefficients, "c", axis=0, tiled=True)
    ny = lax.axis_size("y")
    stack, lo = ring(x, "y")
    want = (jnp.arange(ny) - lax.axis_index("y") - lo) % ny
    x = jnp.take(stack, want, axis=0).reshape(-1, NMO)
    stack, lo = ring(x, "z")
    per = NSH // lax.axis_size("z")
    return stack.reshape(-1, NMO), per * (lax.axis_index("z") + lo)


def body(integrals, coefficients, tile_blocks, block_owner):
    groups = lax.axis_size("grp")
    whole_coef, shift = gather_coef(coefficients)
    panels = whole_coef.reshape(NSH, SB, NMO)
    tiles = integrals[0, 0]
    blocks = (tile_blocks[0, 0] - shift) % NSH
    la_coef = jnp.take(panels, blocks[:, 0], axis=0)
    si_coef = jnp.take(panels, blocks[:, 1], axis=0)
    quarter = jnp.einsum(
        "trab,tbj->tarj", tiles, si_coef, preferred_element_type=jnp.float32
    ).astype(jnp.bfloat16)
    half = jnp.einsum("tai,tarj->irj", la_coef, quarter, preferred_element_type=jnp.float32).astype(
        jnp.bfloat16
    )
    pair_blocks = half.reshape(IJB, IPB, R, NMO)
    source, filled = slot_table(block_owner, groups, CAP)
    picked = jnp.take(pair_blocks, source, axis=0)
    picked = jnp.where(filled[:, None, None, None], picked, jnp.zeros_like(picked))
    return lax.all_to_all(picked[:, None], "grp", 0, 1, tiled=True)


def solution(mesh):
    nblk = mesh.shape["blk"]
    devs = np.asarray(mesh.devices).reshape(mesh.shape["grp"], nblk // 8, 4, 2)
    parts = Mesh(devs, ("grp",) + BLK)
    in_specs = (
        P("grp", BLK, None, None, None, None),
        P(BLK, None),
        P("grp", BLK, None, None),
        P(),
    )
    out_specs = P("grp", None, None, BLK, None)
    return jax.shard_map(body, mesh=parts, in_specs=in_specs, out_specs=out_specs, check_vma=False)
```

```python
import numpy as np
import jax
import jax.numpy as jnp
from jax import lax
from jax.sharding import Mesh, PartitionSpec as P

NMO = 192
SB = 128
NSH = 24
R = 24
IJB = 48
CAP = 24
IPB = 4

BLK = ("z", "y", "c")


def slot_table(block_owner, groups, capacity):
    count = block_owner.shape[0]
    order = jnp.arange(count, dtype=jnp.int32)
    same = block_owner[:, None] == block_owner[None, :]
    earlier = order[None, :] < order[:, None]
    rank = jnp.sum((same & earlier).astype(jnp.int32), axis=1)
    slot = block_owner * capacity + rank
    slots = jnp.arange(groups * capacity, dtype=jnp.int32)
    match = slot[None, :] == slots[:, None]
    source = jnp.sum(jnp.where(match, order[None, :], 0), axis=1)
    filled = jnp.any(match, axis=1)
    return (source, filled)


def ring(x, axis):
    n = lax.axis_size(axis)
    got = {0: x}
    f = x
    for k in range(1, n // 2 + 1):
        f = lax.ppermute(f, axis, [(s, (s + 1) % n) for s in range(n)])
        got[-k] = f
    b = x
    for k in range(1, n - n // 2):
        b = lax.ppermute(b, axis, [(s, (s - 1) % n) for s in range(n)])
        got[k] = b
    lo = -(n // 2)
    return jnp.stack([got[o] for o in range(lo, lo + n)]), lo


def gather_coef(coefficients):
    x = lax.all_gather(coefficients, "c", axis=0, tiled=True)
    ny = lax.axis_size("y")
    stack, lo = ring(x, "y")
    want = (jnp.arange(ny) - lax.axis_index("y") - lo) % ny
    x = jnp.take(stack, want, axis=0).reshape(-1, NMO)
    stack, lo = ring(x, "z")
    per = NSH // lax.axis_size("z")
    return stack.reshape(-1, NMO), per * (lax.axis_index("z") + lo)


def body(integrals, coefficients, tile_blocks, block_owner):
    groups = lax.axis_size("grp")
    whole_coef, shift = gather_coef(coefficients)
    panels = whole_coef.reshape(NSH, SB, NMO)
    tiles = integrals[0, 0]
    blocks = (tile_blocks[0, 0] - shift) % NSH
    la_coef = jnp.take(panels, blocks[:, 0], axis=0, mode="clip")
    si_coef = jnp.take(panels, blocks[:, 1], axis=0, mode="clip")
    la_coef = jnp.pad(la_coef, ((0, 0), (0, 0), (0, IPB)))
    quarter = jnp.einsum(
        "trab,tbj->tarj", tiles, si_coef, preferred_element_type=jnp.float32
    ).astype(jnp.bfloat16)
    half = jnp.einsum("tai,tarj->irj", la_coef, quarter, preferred_element_type=jnp.float32).astype(
        jnp.bfloat16
    )
    pair_blocks = half.reshape(IJB + 1, IPB, R, NMO)
    source, filled = slot_table(block_owner, groups, CAP)
    source = jnp.where(filled, source, IJB)
    picked = jnp.take(pair_blocks, source, axis=0, mode="clip")
    return lax.all_to_all(picked[:, None], "grp", 0, 1, tiled=True)


def solution(mesh):
    nblk = mesh.shape["blk"]
    devs = np.asarray(mesh.devices).reshape(mesh.shape["grp"], nblk // 8, 4, 2)
    parts = Mesh(devs, ("grp",) + BLK)
    in_specs = (
        P("grp", BLK, None, None, None, None),
        P(BLK, None),
        P("grp", BLK, None, None),
        P(),
    )
    out_specs = P("grp", None, None, BLK, None)
    return jax.shard_map(body, mesh=parts, in_specs=in_specs, out_specs=out_specs, check_vma=False)
```

```python
import numpy as np
import jax
import jax.numpy as jnp
from jax import lax
from jax.sharding import Mesh, PartitionSpec as P

NMO = 192
SB = 128
NSH = 24
R = 24
IJB = 48
CAP = 24
IPB = 4

BLK = ("z", "y", "c")


def slot_table(block_owner, groups, capacity):
    count = block_owner.shape[0]
    order = jnp.arange(count, dtype=jnp.int32)
    same = block_owner[:, None] == block_owner[None, :]
    earlier = order[None, :] < order[:, None]
    rank = jnp.sum((same & earlier).astype(jnp.int32), axis=1)
    slot = block_owner * capacity + rank
    slots = jnp.arange(groups * capacity, dtype=jnp.int32)
    match = slot[None, :] == slots[:, None]
    source = jnp.sum(jnp.where(match, order[None, :], 0), axis=1)
    filled = jnp.any(match, axis=1)
    return (source, filled)


def ring(x, axis):
    n = lax.axis_size(axis)
    got = {0: x}
    f = x
    for k in range(1, n // 2 + 1):
        f = lax.ppermute(f, axis, [(s, (s + 1) % n) for s in range(n)])
        got[-k] = f
    b = x
    for k in range(1, n - n // 2):
        b = lax.ppermute(b, axis, [(s, (s - 1) % n) for s in range(n)])
        got[k] = b
    lo = -(n // 2)
    return jnp.stack([got[o] for o in range(lo, lo + n)]), lo


def direct(x, axis):
    n = lax.axis_size(axis)
    got = [x] + [lax.ppermute(x, axis, [(s, (s + o) % n) for s in range(n)]) for o in range(1, n)]
    stack = jnp.stack(got)
    want = (lax.axis_index(axis) - jnp.arange(n)) % n
    return jnp.take(stack, want, axis=0, mode="clip")


def gather_coef(coefficients):
    x = lax.all_gather(coefficients, "c", axis=0, tiled=True)
    x = direct(x, "y").reshape(-1, NMO)
    stack, lo = ring(x, "z")
    per = NSH // lax.axis_size("z")
    return stack.reshape(-1, NMO), per * (lax.axis_index("z") + lo)


def body(integrals, coefficients, tile_blocks, block_owner):
    groups = lax.axis_size("grp")
    whole_coef, shift = gather_coef(coefficients)
    panels = whole_coef.reshape(NSH, SB, NMO)
    tiles = integrals[0, 0]
    blocks = (tile_blocks[0, 0] - shift) % NSH
    la_coef = jnp.take(panels, blocks[:, 0], axis=0, mode="clip")
    si_coef = jnp.take(panels, blocks[:, 1], axis=0, mode="clip")
    la_coef = jnp.pad(la_coef, ((0, 0), (0, 0), (0, IPB)))
    quarter = jnp.einsum(
        "trab,tbj->tarj", tiles, si_coef, preferred_element_type=jnp.float32
    ).astype(jnp.bfloat16)
    half = jnp.einsum("tai,tarj->irj", la_coef, quarter, preferred_element_type=jnp.float32).astype(
        jnp.bfloat16
    )
    pair_blocks = half.reshape(IJB + 1, IPB, R, NMO)
    source, filled = slot_table(block_owner, groups, CAP)
    source = jnp.where(filled, source, IJB)
    picked = jnp.take(pair_blocks, source, axis=0, mode="clip")
    return lax.all_to_all(picked[:, None], "grp", 0, 1, tiled=True)


def solution(mesh):
    nblk = mesh.shape["blk"]
    devs = np.asarray(mesh.devices).reshape(mesh.shape["grp"], nblk // 8, 4, 2)
    parts = Mesh(devs, ("grp",) + BLK)
    in_specs = (
        P("grp", BLK, None, None, None, None),
        P(BLK, None),
        P("grp", BLK, None, None),
        P(),
    )
    out_specs = P("grp", None, None, BLK, None)
    return jax.shard_map(body, mesh=parts, in_specs=in_specs, out_specs=out_specs, check_vma=False)
```

```python
import numpy as np
import jax
import jax.numpy as jnp
from jax import lax
from jax.sharding import Mesh, PartitionSpec as P

NMO = 192
SB = 128
NSH = 24
R = 24
IJB = 48
CAP = 24
IPB = 4

BLK = ("z", "y", "c")


def slot_table(block_owner, groups, capacity):
    count = block_owner.shape[0]
    order = jnp.arange(count, dtype=jnp.int32)
    same = block_owner[:, None] == block_owner[None, :]
    earlier = order[None, :] < order[:, None]
    rank = jnp.sum((same & earlier).astype(jnp.int32), axis=1)
    slot = block_owner * capacity + rank
    slots = jnp.arange(groups * capacity, dtype=jnp.int32)
    match = slot[None, :] == slots[:, None]
    source = jnp.sum(jnp.where(match, order[None, :], 0), axis=1)
    filled = jnp.any(match, axis=1)
    return (source, filled)


def ring(x, axis):
    n = lax.axis_size(axis)
    got = {0: x}
    f = x
    for k in range(1, n // 2 + 1):
        f = lax.ppermute(f, axis, [(s, (s + 1) % n) for s in range(n)])
        got[-k] = f
    b = x
    for k in range(1, n - n // 2):
        b = lax.ppermute(b, axis, [(s, (s - 1) % n) for s in range(n)])
        got[k] = b
    lo = -(n // 2)
    return jnp.stack([got[o] for o in range(lo, lo + n)]), lo


def direct(x, axis):
    n = lax.axis_size(axis)
    got = [x] + [lax.ppermute(x, axis, [(s, (s + o) % n) for s in range(n)]) for o in range(1, n)]
    stack = jnp.stack(got)
    want = (lax.axis_index(axis) - jnp.arange(n)) % n
    return jnp.take(stack, want, axis=0, mode="clip")


def zring8(x):
    nz = lax.axis_size("z")
    zc = ("z", "c")

    def at(z, c):
        return (z % nz) * 2 + c

    f1 = lax.ppermute(x, zc, [(at(z, 0), at(z + 1, 0)) for z in range(nz)] + [(at(z, 1), at(z + 2, 1)) for z in range(nz)])
    b1 = lax.ppermute(x, zc, [(at(z, 0), at(z - 1, 0)) for z in range(nz)] + [(at(z, 1), at(z - 2, 1)) for z in range(nz)])
    pa = lax.ppermute(f1, zc, [(at(z, 1), at(z + 1, 0)) for z in range(nz)])
    pb = lax.ppermute(f1, zc, [(at(z, 1), at(z + 2, 1)) for z in range(nz)])
    pc = lax.ppermute(b1, zc, [(at(z, 1), at(z - 1, 0)) for z in range(nz)])
    first = lax.axis_index("c") == 0
    mine = jnp.stack([f1, b1, jnp.where(first, pa, pb), pc])
    theirs = lax.ppermute(mine, "c", [(0, 1), (1, 0)])
    a = jnp.where(first, mine, theirs)
    b = jnp.where(first, theirs, mine)
    return jnp.concatenate([b[2], a[2], b[0], a[0], x, a[1], b[1], a[3]], axis=0), -4


def gather_coef(coefficients):
    x = lax.all_gather(coefficients, "c", axis=0, tiled=True)
    x = direct(x, "y").reshape(-1, NMO)
    if lax.axis_size("z") == 8:
        rows, lo = zring8(x)
    else:
        stack, lo = ring(x, "z")
        rows = stack.reshape(-1, NMO)
    per = NSH // lax.axis_size("z")
    return rows, per * (lax.axis_index("z") + lo)


def body(integrals, coefficients, tile_blocks, block_owner):
    groups = lax.axis_size("grp")
    whole_coef, shift = gather_coef(coefficients)
    panels = whole_coef.reshape(NSH, SB, NMO)
    tiles = integrals[0, 0]
    blocks = (tile_blocks[0, 0] - shift) % NSH
    la_coef = jnp.take(panels, blocks[:, 0], axis=0, mode="clip")
    si_coef = jnp.take(panels, blocks[:, 1], axis=0, mode="clip")
    la_coef = jnp.pad(la_coef, ((0, 0), (0, 0), (0, IPB)))
    quarter = jnp.einsum(
        "trab,tbj->tarj", tiles, si_coef, preferred_element_type=jnp.float32
    ).astype(jnp.bfloat16)
    half = jnp.einsum("tai,tarj->irj", la_coef, quarter, preferred_element_type=jnp.float32).astype(
        jnp.bfloat16
    )
    pair_blocks = half.reshape(IJB + 1, IPB, R, NMO)
    source, filled = slot_table(block_owner, groups, CAP)
    source = jnp.where(filled, source, IJB)
    picked = jnp.take(pair_blocks, source, axis=0, mode="clip")
    return lax.all_to_all(picked[:, None], "grp", 0, 1, tiled=True)


def solution(mesh):
    nblk = mesh.shape["blk"]
    devs = np.asarray(mesh.devices).reshape(mesh.shape["grp"], nblk // 8, 4, 2)
    parts = Mesh(devs, ("grp",) + BLK)
    in_specs = (
        P("grp", BLK, None, None, None, None),
        P(BLK, None),
        P("grp", BLK, None, None),
        P(),
    )
    out_specs = P("grp", None, None, BLK, None)
    return jax.shard_map(body, mesh=parts, in_specs=in_specs, out_specs=out_specs, check_vma=False)
```

```python
import numpy as np
import jax
import jax.numpy as jnp
from jax import lax
from jax.sharding import Mesh, PartitionSpec as P

NMO = 192
SB = 128
NSH = 24
R = 24
IJB = 48
CAP = 24
IPB = 4

BLK = ("z", "y", "c")


def slot_table(block_owner, groups, capacity):
    count = block_owner.shape[0]
    order = jnp.arange(count, dtype=jnp.int32)
    same = block_owner[:, None] == block_owner[None, :]
    earlier = order[None, :] < order[:, None]
    rank = jnp.sum((same & earlier).astype(jnp.int32), axis=1)
    slot = block_owner * capacity + rank
    slots = jnp.arange(groups * capacity, dtype=jnp.int32)
    match = slot[None, :] == slots[:, None]
    source = jnp.sum(jnp.where(match, order[None, :], 0), axis=1)
    filled = jnp.any(match, axis=1)
    return (source, filled)


def ring(x, axis):
    n = lax.axis_size(axis)
    got = {0: x}
    f = x
    for k in range(1, n // 2 + 1):
        f = lax.ppermute(f, axis, [(s, (s + 1) % n) for s in range(n)])
        got[-k] = f
    b = x
    for k in range(1, n - n // 2):
        b = lax.ppermute(b, axis, [(s, (s - 1) % n) for s in range(n)])
        got[k] = b
    lo = -(n // 2)
    return jnp.stack([got[o] for o in range(lo, lo + n)]), lo


def direct(x, axis):
    n = lax.axis_size(axis)
    got = [x] + [lax.ppermute(x, axis, [(s, (s + o) % n) for s in range(n)]) for o in range(1, n)]
    stack = jnp.stack(got)
    want = (lax.axis_index(axis) - jnp.arange(n)) % n
    return jnp.take(stack, want, axis=0, mode="clip")


def zring8(x):
    nz = lax.axis_size("z")
    zc = ("z", "c")

    def at(z, c):
        return (z % nz) * 2 + c

    f1 = lax.ppermute(x, zc, [(at(z, 0), at(z + 1, 0)) for z in range(nz)] + [(at(z, 1), at(z + 2, 1)) for z in range(nz)])
    b1 = lax.ppermute(x, zc, [(at(z, 0), at(z - 1, 0)) for z in range(nz)] + [(at(z, 1), at(z - 2, 1)) for z in range(nz)])
    pa = lax.ppermute(f1, zc, [(at(z, 1), at(z + 1, 0)) for z in range(nz)])
    cut = x.shape[0] // 2
    pb = jnp.concatenate([
        lax.ppermute(f1[:cut], zc, [(at(z, 1), at(z + 2, 1)) for z in range(nz)]),
        lax.ppermute(b1[cut:], zc, [(at(z, 1), at(z - 2, 1)) for z in range(nz)]),
    ], axis=0)
    pc = lax.ppermute(b1, zc, [(at(z, 1), at(z - 1, 0)) for z in range(nz)])
    first = lax.axis_index("c") == 0
    mine = jnp.stack([f1, b1, jnp.where(first, pa, pb), pc])
    theirs = lax.ppermute(mine, "c", [(0, 1), (1, 0)])
    a = jnp.where(first, mine, theirs)
    b = jnp.where(first, theirs, mine)
    return jnp.concatenate([b[2], a[2], b[0], a[0], x, a[1], b[1], a[3]], axis=0), -4


def gather_coef(coefficients):
    x = lax.all_gather(coefficients, "c", axis=0, tiled=True)
    x = direct(x, "y").reshape(-1, NMO)
    if lax.axis_size("z") == 8:
        rows, lo = zring8(x)
    else:
        stack, lo = ring(x, "z")
        rows = stack.reshape(-1, NMO)
    per = NSH // lax.axis_size("z")
    return rows, per * (lax.axis_index("z") + lo)


def body(integrals, coefficients, tile_blocks, block_owner):
    groups = lax.axis_size("grp")
    whole_coef, shift = gather_coef(coefficients)
    panels = whole_coef.reshape(NSH, SB, NMO)
    tiles = integrals[0, 0]
    blocks = (tile_blocks[0, 0] - shift) % NSH
    la_coef = jnp.take(panels, blocks[:, 0], axis=0, mode="clip")
    si_coef = jnp.take(panels, blocks[:, 1], axis=0, mode="clip")
    la_coef = jnp.pad(la_coef, ((0, 0), (0, 0), (0, IPB)))
    quarter = jnp.einsum(
        "trab,tbj->tarj", tiles, si_coef, preferred_element_type=jnp.float32
    ).astype(jnp.bfloat16)
    half = jnp.einsum("tai,tarj->irj", la_coef, quarter, preferred_element_type=jnp.float32).astype(
        jnp.bfloat16
    )
    pair_blocks = half.reshape(IJB + 1, IPB, R, NMO)
    source, filled = slot_table(block_owner, groups, CAP)
    source = jnp.where(filled, source, IJB)
    picked = jnp.take(pair_blocks, source, axis=0, mode="clip")
    return lax.all_to_all(picked[:, None], "grp", 0, 1, tiled=True)


def solution(mesh):
    nblk = mesh.shape["blk"]
    devs = np.asarray(mesh.devices).reshape(mesh.shape["grp"], nblk // 8, 4, 2)
    parts = Mesh(devs, ("grp",) + BLK)
    in_specs = (
        P("grp", BLK, None, None, None, None),
        P(BLK, None),
        P("grp", BLK, None, None),
        P(),
    )
    out_specs = P("grp", None, None, BLK, None)
    return jax.shard_map(body, mesh=parts, in_specs=in_specs, out_specs=out_specs, check_vma=False)
```

```python
import numpy as np
import jax
import jax.numpy as jnp
from jax import lax
from jax.sharding import Mesh, PartitionSpec as P

NMO = 192
SB = 128
NSH = 24
R = 24
IJB = 48
CAP = 24
IPB = 4

BLK = ("z", "y", "c")


def slot_table(block_owner, groups, capacity):
    count = block_owner.shape[0]
    order = jnp.arange(count, dtype=jnp.int32)
    same = block_owner[:, None] == block_owner[None, :]
    earlier = order[None, :] < order[:, None]
    rank = jnp.sum((same & earlier).astype(jnp.int32), axis=1)
    slot = block_owner * capacity + rank
    slots = jnp.arange(groups * capacity, dtype=jnp.int32)
    match = slot[None, :] == slots[:, None]
    source = jnp.sum(jnp.where(match, order[None, :], 0), axis=1)
    filled = jnp.any(match, axis=1)
    return (source, filled)


def ring(x, axis):
    n = lax.axis_size(axis)
    got = {0: x}
    f = x
    for k in range(1, n // 2 + 1):
        f = lax.ppermute(f, axis, [(s, (s + 1) % n) for s in range(n)])
        got[-k] = f
    b = x
    for k in range(1, n - n // 2):
        b = lax.ppermute(b, axis, [(s, (s - 1) % n) for s in range(n)])
        got[k] = b
    lo = -(n // 2)
    return jnp.stack([got[o] for o in range(lo, lo + n)]), lo


def direct(x, axis):
    n = lax.axis_size(axis)
    got = [x] + [lax.ppermute(x, axis, [(s, (s + o) % n) for s in range(n)]) for o in range(1, n)]
    stack = jnp.stack(got)
    want = (lax.axis_index(axis) - jnp.arange(n)) % n
    return jnp.take(stack, want, axis=0, mode="clip")


def zring8(x):
    nz = lax.axis_size("z")
    zc = ("z", "c")

    def at(z, c):
        return (z % nz) * 2 + c

    f1 = lax.ppermute(x, zc, [(at(z, 0), at(z + 1, 0)) for z in range(nz)] + [(at(z, 1), at(z + 2, 1)) for z in range(nz)])
    b1 = lax.ppermute(x, zc, [(at(z, 0), at(z - 1, 0)) for z in range(nz)] + [(at(z, 1), at(z - 2, 1)) for z in range(nz)])
    pa = lax.ppermute(f1, zc, [(at(z, 1), at(z + 1, 0)) for z in range(nz)])
    pb = lax.ppermute(f1, zc, [(at(z, 1), at(z + 2, 1)) for z in range(nz)])
    pc = lax.ppermute(b1, zc, [(at(z, 1), at(z - 1, 0)) for z in range(nz)])
    first = lax.axis_index("c") == 0
    mine = jnp.stack([f1, b1, jnp.where(first, pa, pb), pc])
    theirs = lax.ppermute(mine, "c", [(0, 1), (1, 0)])
    a = jnp.where(first, mine, theirs)
    b = jnp.where(first, theirs, mine)
    return jnp.concatenate([b[2], a[2], b[0], a[0], x, a[1], b[1], a[3]], axis=0), -4


def gather_coef(coefficients):
    mine = direct(coefficients, "y")
    theirs = lax.ppermute(mine, "c", [(0, 1), (1, 0)])
    first = lax.axis_index("c") == 0
    x = jnp.stack([jnp.where(first, mine, theirs), jnp.where(first, theirs, mine)], axis=1).reshape(-1, NMO)
    if lax.axis_size("z") == 8:
        rows, lo = zring8(x)
    else:
        stack, lo = ring(x, "z")
        rows = stack.reshape(-1, NMO)
    per = NSH // lax.axis_size("z")
    return rows, per * (lax.axis_index("z") + lo)


def body(integrals, coefficients, tile_blocks, block_owner):
    groups = lax.axis_size("grp")
    whole_coef, shift = gather_coef(coefficients)
    panels = whole_coef.reshape(NSH, SB, NMO)
    tiles = integrals[0, 0]
    blocks = (tile_blocks[0, 0] - shift) % NSH
    la_coef = jnp.take(panels, blocks[:, 0], axis=0, mode="clip")
    si_coef = jnp.take(panels, blocks[:, 1], axis=0, mode="clip")
    la_coef = jnp.pad(la_coef, ((0, 0), (0, 0), (0, IPB)))
    quarter = jnp.einsum(
        "trab,tbj->tarj", tiles, si_coef, preferred_element_type=jnp.float32
    ).astype(jnp.bfloat16)
    half = jnp.einsum("tai,tarj->irj", la_coef, quarter, preferred_element_type=jnp.float32).astype(
        jnp.bfloat16
    )
    pair_blocks = half.reshape(IJB + 1, IPB, R, NMO)
    source, filled = slot_table(block_owner, groups, CAP)
    source = jnp.where(filled, source, IJB)
    picked = jnp.take(pair_blocks, source, axis=0, mode="clip")
    return lax.all_to_all(picked[:, None], "grp", 0, 1, tiled=True)


def solution(mesh):
    nblk = mesh.shape["blk"]
    devs = np.asarray(mesh.devices).reshape(mesh.shape["grp"], nblk // 8, 4, 2)
    parts = Mesh(devs, ("grp",) + BLK)
    in_specs = (
        P("grp", BLK, None, None, None, None),
        P(BLK, None),
        P("grp", BLK, None, None),
        P(),
    )
    out_specs = P("grp", None, None, BLK, None)
    return jax.shard_map(body, mesh=parts, in_specs=in_specs, out_specs=out_specs, check_vma=False)
```

```python
import numpy as np
import jax
import jax.numpy as jnp
from jax import lax
from jax.sharding import Mesh, PartitionSpec as P

NMO = 192
SB = 128
NSH = 24
R = 24
IJB = 48
CAP = 24
IPB = 4

BLK = ("z", "y", "c")


def slot_table(block_owner, groups, capacity):
    count = block_owner.shape[0]
    order = jnp.arange(count, dtype=jnp.int32)
    same = block_owner[:, None] == block_owner[None, :]
    earlier = order[None, :] < order[:, None]
    rank = jnp.sum((same & earlier).astype(jnp.int32), axis=1)
    slot = block_owner * capacity + rank
    slots = jnp.arange(groups * capacity, dtype=jnp.int32)
    match = slot[None, :] == slots[:, None]
    source = jnp.sum(jnp.where(match, order[None, :], 0), axis=1)
    filled = jnp.any(match, axis=1)
    return (source, filled)


def ring(x, axis):
    n = lax.axis_size(axis)
    got = {0: x}
    f = x
    for k in range(1, n // 2 + 1):
        f = lax.ppermute(f, axis, [(s, (s + 1) % n) for s in range(n)])
        got[-k] = f
    b = x
    for k in range(1, n - n // 2):
        b = lax.ppermute(b, axis, [(s, (s - 1) % n) for s in range(n)])
        got[k] = b
    lo = -(n // 2)
    return jnp.stack([got[o] for o in range(lo, lo + n)]), lo


def direct(x, axis):
    n = lax.axis_size(axis)
    got = [x] + [lax.ppermute(x, axis, [(s, (s + o) % n) for s in range(n)]) for o in range(1, n)]
    stack = jnp.stack(got)
    want = (lax.axis_index(axis) - jnp.arange(n)) % n
    return jnp.take(stack, want, axis=0, mode="clip")


def zring8(x):
    nz = lax.axis_size("z")
    zc = ("z", "c")

    def at(z, c):
        return (z % nz) * 2 + (1 - c)

    f1 = lax.ppermute(x, zc, [(at(z, 0), at(z + 1, 0)) for z in range(nz)] + [(at(z, 1), at(z + 2, 1)) for z in range(nz)])
    b1 = lax.ppermute(x, zc, [(at(z, 0), at(z - 1, 0)) for z in range(nz)] + [(at(z, 1), at(z - 2, 1)) for z in range(nz)])
    pa = lax.ppermute(f1, zc, [(at(z, 1), at(z + 1, 0)) for z in range(nz)])
    pb = lax.ppermute(f1, zc, [(at(z, 1), at(z + 2, 1)) for z in range(nz)])
    pc = lax.ppermute(b1, zc, [(at(z, 1), at(z - 1, 0)) for z in range(nz)])
    first = lax.axis_index("c") == 1
    mine = jnp.stack([f1, b1, jnp.where(first, pa, pb), pc])
    theirs = lax.ppermute(mine, "c", [(0, 1), (1, 0)])
    a = jnp.where(first, mine, theirs)
    b = jnp.where(first, theirs, mine)
    return jnp.concatenate([b[2], a[2], b[0], a[0], x, a[1], b[1], a[3]], axis=0), -4


def gather_coef(coefficients):
    x = lax.all_gather(coefficients, "c", axis=0, tiled=True)
    x = direct(x, "y").reshape(-1, NMO)
    if lax.axis_size("z") == 8:
        rows, lo = zring8(x)
    else:
        stack, lo = ring(x, "z")
        rows = stack.reshape(-1, NMO)
    per = NSH // lax.axis_size("z")
    return rows, per * (lax.axis_index("z") + lo)


def body(integrals, coefficients, tile_blocks, block_owner):
    groups = lax.axis_size("grp")
    whole_coef, shift = gather_coef(coefficients)
    panels = whole_coef.reshape(NSH, SB, NMO)
    tiles = integrals[0, 0]
    blocks = (tile_blocks[0, 0] - shift) % NSH
    la_coef = jnp.take(panels, blocks[:, 0], axis=0, mode="clip")
    si_coef = jnp.take(panels, blocks[:, 1], axis=0, mode="clip")
    la_coef = jnp.pad(la_coef, ((0, 0), (0, 0), (0, IPB)))
    quarter = jnp.einsum(
        "trab,tbj->tarj", tiles, si_coef, preferred_element_type=jnp.float32
    ).astype(jnp.bfloat16)
    half = jnp.einsum("tai,tarj->irj", la_coef, quarter, preferred_element_type=jnp.float32).astype(
        jnp.bfloat16
    )
    pair_blocks = half.reshape(IJB + 1, IPB, R, NMO)
    source, filled = slot_table(block_owner, groups, CAP)
    source = jnp.where(filled, source, IJB)
    picked = jnp.take(pair_blocks, source, axis=0, mode="clip")
    return lax.all_to_all(picked[:, None], "grp", 0, 1, tiled=True)


def solution(mesh):
    nblk = mesh.shape["blk"]
    devs = np.asarray(mesh.devices).reshape(mesh.shape["grp"], nblk // 8, 4, 2)
    parts = Mesh(devs, ("grp",) + BLK)
    in_specs = (
        P("grp", BLK, None, None, None, None),
        P(BLK, None),
        P("grp", BLK, None, None),
        P(),
    )
    out_specs = P("grp", None, None, BLK, None)
    return jax.shard_map(body, mesh=parts, in_specs=in_specs, out_specs=out_specs, check_vma=False)
```
